256 devices in a mesh: rep: 4 (over z_hi, core), ep: 64 (over z_lo, y, x).
Axes of the slice: x: 4, y: 4, z: 8 (z_hi: 2, z_lo: 4; z = z_hi * 4 + z_lo), core: 2. Of those that a mesh axis runs over, the one named last changes fastest.
Arguments:
- tokens: bfloat16 [4096, 3584], P('ep', 'rep'), may hold values from -6 to 6
- route_ids: int32 [4096, 8], P('ep'), may hold values from 0 to 127, all different within a row; in each aligned block of 64 rows (0 to 63, 64 to 127, ...) at most 6 rows name the same one
- route_weights: float32 [4096, 8], P('ep'), may hold values from 0.05 to 0.5
- swap_plan: int32 [64, 2], replicated, may hold values from 0 to 63, as said below
- gate_up: bfloat16 [128, 3584, 2, 1024], P('ep', None, None, 'rep'), may hold values from -0.09375 to 0.09375
- down: bfloat16 [128, 1024, 3584], P('ep', 'rep'), may hold values from -0.1875 to 0.1875
Outputs:
- mixed: bfloat16 [4096, 3584], P('ep', 'rep')
The draws below stay inside these ranges and needn't reach their ends.
Inputs may be any that keep to these rules, and one draw needn't show every extreme that they name: swap_plan[d, 0] is d or the index 32 away from d (d + 64 / 2 modulo 64), and the pairing is mutual; swap_plan[d, 1] is a local slot below 2; at least one pair swaps. `route_ids`: each row names 8 different slots; among the rows of one index of ep no slot is named by more than 6 rows, a bound that some blocks reach.
All inputs are finite; a program needn't handle non-finite values.
Results may differ from the reference program's by a relative error of at most 0.012.
Values may be sent and summed in bfloat16 or wider, within the bound.
No kernel may reach another device: no remote copies, remote signals or barrier semaphores. Data moves between devices by JAX's collectives and lax.ppermute only.
A program may use at most 128 MiB of HBM per device.

```python
import math
import jax
import jax.numpy as jnp
import numpy as np
from jax import lax

D = 3584
FF = 1024
TOP = 8
EXP_DEV = 2
TOK_DEV = 64
EXPERTS = 128
TOKENS = 4096
CAP = 6
N_REP = 4
N_EP = 64


def draw_swap_plan(key, part):
    first_key, second_key = jax.random.split(key)
    half_way = N_EP // 2
    flags = jax.random.randint(first_key, (half_way,), 0, 2).astype(jnp.int32)
    flags = flags.at[0].set(1)
    devices = jnp.arange(N_EP, dtype=jnp.int32)
    pair_flag = flags[devices % half_way]
    across = jnp.where(devices < half_way, devices + half_way, devices - half_way)
    partner = jnp.where(pair_flag == 1, across, devices)
    given_slot = jax.random.randint(second_key, (N_EP,), 0, EXP_DEV).astype(jnp.int32)
    return jnp.stack([partner, given_slot], axis=1).astype(jnp.int32)


def block_scale(key, extent, cuts, low, largest):
    loudness = 1.0
    for dim, parts in cuts:
        steps = jax.random.uniform(jax.random.fold_in(jax.random.fold_in(key, 6), dim), (parts,), jnp.float32, low / len(cuts), largest / len(cuts))
        loudness = loudness * jnp.repeat(jnp.exp(steps), extent[dim] // parts).reshape((-1,) + (1,) * (len(extent) - 1 - dim))
    return loudness


def assign_block(rng, own, number, rows, number_of, top, most, skew):
    ranking = jax.random.permutation(rng, number_of)
    crowded, usual = portions_of(number_of, rows * top, most, skew, True), portions_of(number_of, rows * top, most, skew, False)
    places = jnp.arange(number_of)

    def named(sizes, turn):
        used = int((sizes > 0).sum())
        fixed = max(1, used // 4)
        passed = fixed + (places - fixed + turn * (used - fixed)) % max(1, number_of - fixed)
        return jnp.zeros((number_of,), jnp.int32).at[ranking[jnp.where(places < fixed, places, passed)]].set(jnp.asarray(sizes, jnp.int32))

    sizes = jnp.where(number % 4 == 0, named(crowded, number // 4), named(usual, number - number // 4 - 1))
    mixed = jax.random.permutation(jax.random.fold_in(own, 3), number_of)
    source_of, sink = mixed[0:number_of // 2 * 2:2], mixed[1:number_of // 2 * 2:2]
    slack = jnp.minimum(sizes[source_of] - 1, most - sizes[sink]) // 2
    slack = jnp.where((source_of == ranking[0]) | (sink == ranking[0]) | (sizes[sink] == 0), 0, jnp.maximum(slack, 0))
    passed = jax.random.randint(jax.random.fold_in(own, 4), (number_of // 2,), 0, 1 << 20) % (slack + 1)
    sizes = sizes.at[source_of].add(-passed).at[sink].add(passed)
    labels = jnp.searchsorted(jnp.cumsum(sizes), jnp.arange(rows * top), side="right").astype(jnp.int32)
    grid = labels.reshape(top, rows).T
    grid = grid[jax.random.permutation(jax.random.fold_in(own, 1), rows)]
    turn = jax.random.randint(jax.random.fold_in(own, 2), (rows, 1), 0, top)
    return jnp.take_along_axis(grid, (jnp.arange(top)[None, :] + turn) % top, axis=1)


def portions_of(amount, total, reach, slope, full):
    loads = [(1 << 20) // math.isqrt(rank ** slope) + 1 for rank in range(1, amount + 1)]
    largest = reach if full else min(reach, max(-(-total // amount), total * loads[0] // sum(loads)))
    least = 1 if total - largest >= amount - 1 else 0
    holding, rest = [largest] + [least] * (amount - 1), total - largest - least * (amount - 1)
    while rest > 0:
        free = [i for i in range(1, amount) if holding[i] < largest] or [i for i in range(1, amount) if holding[i] < reach]
        mass, budget = sum([loads[i] for i in free]), rest
        for i in free:
            more = min(reach - holding[i], max(1, budget * loads[i] // mass), rest)
            holding[i] = holding[i] + more
            rest = rest - more
    return np.array(holding)


def normal_values(rng, extent, deviation, limit, shards=(), held_as=jnp.bfloat16):
    loudness = block_scale(rng, extent, shards, -0.22, 0.18) if shards else 1.0
    array = jax.random.normal(rng, extent, jnp.float32) * deviation * loudness
    return jnp.minimum(jnp.maximum(array, -limit), limit).astype(held_as)


def setup_inputs(seed: int = 0) -> dict:
    key_list = jax.random.split(jax.random.key(seed), 7)
    tokens = normal_values(key_list[0], (TOKENS, D), 1.0, 6.0, ((0, 64), (1, 4)))
    route_ids_keys = jax.random.split(jax.random.fold_in(key_list[1], 1), TOKENS // TOK_DEV)
    route_ids_turns = jax.random.permutation(jax.random.fold_in(key_list[1], 3), TOKENS // TOK_DEV)
    route_ids = jax.vmap(lambda own, number: assign_block(jax.random.fold_in(key_list[1], 2), own, number, TOK_DEV, EXPERTS, TOP, CAP, 2))(route_ids_keys, route_ids_turns).reshape((TOKENS, TOP))
    route_weights = jnp.clip(jnp.exp(math.log(0.5) - 2.3025851 * jax.random.uniform(key_list[2], (TOKENS, TOP), jnp.float32) ** block_scale(key_list[2], (TOKENS, TOP), ((0, 64),), -0.2, 0.2)), 0.05, 0.5)
    swap_plan = draw_swap_plan(jax.random.fold_in(key_list[6], 71), 0)
    gate_up = normal_values(key_list[4], (EXPERTS, D, 2, FF), D ** -0.5, 0.09375, ((0, 64), (3, 4)))
    down = normal_values(key_list[5], (EXPERTS, FF, D), FF ** -0.5, 0.1875, ((0, 64), (1, 4)))
    return {"tokens": tokens, "route_ids": route_ids, "route_weights": route_weights, "swap_plan": swap_plan, "gate_up": gate_up, "down": down}


def holder_table(swap_plan):
    devices = jnp.arange(N_EP, dtype=jnp.int32)
    half_way = N_EP // 2
    partner = swap_plan[:, 0].astype(jnp.int32)
    given_slot = swap_plan[:, 1].astype(jnp.int32)
    active = partner != devices
    partner_slot = jnp.where(active, jnp.roll(given_slot, half_way), given_slot)
    slot_ids = jnp.arange(EXPERTS, dtype=jnp.int32)
    local_slot = slot_ids % EXP_DEV
    is_moved = jnp.repeat(active, EXP_DEV) & (local_slot == jnp.repeat(given_slot, EXP_DEV))
    return jnp.where(is_moved, jnp.repeat(partner * EXP_DEV + partner_slot, EXP_DEV), slot_ids).astype(jnp.int32)


def reference(tokens, route_ids, route_weights, swap_plan, gate_up, down):
    holder = holder_table(swap_plan)
    routed = TOKENS * TOP
    flat_ids = route_ids.reshape(routed).astype(jnp.int32)
    owners = holder[flat_ids].astype(jnp.int32)
    ordering = jnp.argsort(owners, stable=True).astype(jnp.int32)
    catalog = jnp.arange(EXPERTS, dtype=jnp.int32)
    counts = jnp.sum((owners[:, None] == catalog[None, :]).astype(jnp.int32), axis=0)
    starts = (jnp.cumsum(counts) - counts).astype(jnp.int32)
    most_rows = N_EP * CAP
    block_width = FF // N_REP

    def per_expert(expert):
        offsets = jnp.arange(most_rows, dtype=jnp.int32)
        picked = starts[expert] + offsets
        is_live = offsets < counts[expert]
        row_ids = ordering[jnp.minimum(picked, routed - 1)]
        features = tokens[row_ids // TOP]
        weights = gate_up[expert]
        gate_part = jnp.dot(features, weights[:, 0, :], preferred_element_type=jnp.float32)
        up_part = jnp.dot(features, weights[:, 1, :], preferred_element_type=jnp.float32)
        hidden = (jax.nn.silu(gate_part) * up_part).astype(jnp.bfloat16)
        running = jnp.zeros((most_rows, D), jnp.float32)
        for block in range(N_REP):
            lo_unit = block * block_width
            part = jnp.dot(hidden[:, lo_unit:lo_unit + block_width], down[expert, lo_unit:lo_unit + block_width, :], preferred_element_type=jnp.float32).astype(jnp.bfloat16)
            running = running + lax.optimization_barrier(part).astype(jnp.float32)
        result = running.astype(jnp.bfloat16)
        target = jnp.where(is_live, row_ids, routed).astype(jnp.int32)
        return result, target

    results, targets = lax.map(per_expert, catalog)
    expert_out = jnp.zeros((routed, D), jnp.bfloat16).at[targets.reshape(-1)].set(results.reshape(-1, D), mode="drop")
    mixed = jnp.sum(expert_out.reshape(TOKENS, TOP, D).astype(jnp.float32) * route_weights[:, :, None], axis=1)
    return mixed.astype(jnp.bfloat16)
```

```python
import jax
import jax.numpy as jnp
from jax import lax
from jax.sharding import PartitionSpec as P


def pair_swap(value, axis, bit):
    return lax.ppermute(value, axis, [(i, i ^ 1 << bit) for i in range(lax.axis_size(axis))])


def pick(flag, first, second):
    return jnp.where(flag, first, second), jnp.where(flag, second, first)


def holder_of(swap_plan, exp_dev):
    ep_size = swap_plan.shape[0]
    slot = jnp.arange(ep_size * exp_dev, dtype=jnp.int32)
    index = slot // exp_dev
    partner = swap_plan[index, 0]
    given = swap_plan[index, 1]
    moved = (partner != index) & (slot % exp_dev == given)
    return jnp.where(moved, partner * exp_dev + swap_plan[partner, 1], slot)


def shards(tokens, route_ids, route_weights, swap_plan, gate_up, down):
    ep_size = lax.axis_size("ep")
    rep = lax.axis_index("rep")
    core = rep % 2
    half = rep // 2
    exp_dev = gate_up.shape[0]
    experts = exp_dev * ep_size
    tok_dev, top_k = route_ids.shape
    routed = tok_dev * top_k
    capacity = max(2, (routed * 3 + 2 * experts - 1) // (2 * experts))
    places = experts * capacity
    width = tokens.shape[1]

    holder = holder_of(swap_plan, exp_dev)
    owners = holder[route_ids.reshape(routed)]
    catalog = jnp.arange(experts, dtype=jnp.int32)
    one_hot = (owners[:, None] == catalog[None, :]).astype(jnp.float32)
    earlier = (jnp.arange(routed)[:, None] > jnp.arange(routed)[None, :]).astype(jnp.float32)
    before = jnp.dot(earlier, one_hot, preferred_element_type=jnp.float32)
    position = jnp.sum(before * one_hot, axis=1).astype(jnp.int32)
    place = owners * capacity + position
    hits = (place[:, None] == jnp.arange(places, dtype=jnp.int32)[None, :]).reshape(tok_dev, top_k, places)
    gather = jnp.sum(hits.astype(jnp.bfloat16), axis=1)
    mixing = jnp.sum(jnp.where(hits, route_weights[:, :, None], 0.0), axis=1)

    other = pair_swap(tokens, "rep", 1)
    low, high = pick(half == 0, tokens, other)
    features = jnp.stack([low, high], axis=1).reshape(tok_dev, 2 * width)
    outgoing = lax.dot_general(
        gather, features, (((0,), (0,)), ((), ())), preferred_element_type=jnp.float32
    ).astype(jnp.bfloat16)
    outgoing = outgoing.reshape(ep_size, exp_dev * capacity, 2 * width)
    arrived = lax.all_to_all(outgoing, "ep", split_axis=0, concat_axis=0, tiled=True)

    mine = arrived.reshape(ep_size, exp_dev * capacity, 2, width)
    theirs = pair_swap(mine, "rep", 0)
    first, second = pick(core == 0, mine, theirs)
    rows = jnp.stack([first, second], axis=3).reshape(ep_size, exp_dev, capacity, 4 * width)

    results = []
    for index in range(exp_dev):
        projected = jnp.einsum(
            "scd,dgf->scgf", rows[:, index], gate_up[index], preferred_element_type=jnp.float32
        )
        hidden = (jax.nn.silu(projected[:, :, 0]) * projected[:, :, 1]).astype(jnp.bfloat16)
        results.append(
            jnp.einsum(
                "scf,fd->scd", hidden, down[index], preferred_element_type=jnp.float32
            ).astype(jnp.bfloat16)
        )
    partial = jnp.stack(results, axis=1).reshape(ep_size, exp_dev * capacity, 2, 2, width)

    keep, send = pick(core == 0, partial[:, :, :, 0], partial[:, :, :, 1])
    paired = (keep.astype(jnp.float32) + pair_swap(send, "rep", 0).astype(jnp.float32)).astype(
        jnp.bfloat16
    )
    returned = lax.all_to_all(
        paired.reshape(ep_size, exp_dev * capacity, 2 * width), "ep", split_axis=0, concat_axis=0, tiled=True
    )
    weighted = jnp.dot(
        mixing,
        returned.reshape(places, 2 * width).astype(jnp.float32),
        precision=lax.Precision.HIGHEST,
        preferred_element_type=jnp.float32,
    ).reshape(tok_dev, 2, width)
    own, away = pick(half == 0, weighted[:, 0], weighted[:, 1])
    return (own + pair_swap(away, "rep", 1)).astype(jnp.bfloat16)


def solution(mesh):
    return jax.shard_map(
        shards,
        mesh=mesh,
        in_specs=(
            P("ep", "rep"),
            P("ep", None),
            P("ep", None),
            P(),
            P("ep", None, None, "rep"),
            P("ep", "rep", None),
        ),
        out_specs=P("ep", "rep"),
        check_vma=False,
    )
```

```python
import jax
import jax.numpy as jnp
import numpy as np
from jax import lax
from jax.sharding import Mesh
from jax.sharding import PartitionSpec as P

EP_AXES = ("z", "y", "x")
PLANE = ("y", "x")


def pair_swap(value, axis, bit):
    return lax.ppermute(value, axis, [(i, i ^ 1 << bit) for i in range(lax.axis_size(axis))])


def pick(flag, first, second):
    return jnp.where(flag, first, second), jnp.where(flag, second, first)


def holder_of(swap_plan, exp_dev):
    ep_size = swap_plan.shape[0]
    slot = jnp.arange(ep_size * exp_dev, dtype=jnp.int32)
    index = slot // exp_dev
    partner = swap_plan[index, 0]
    given = swap_plan[index, 1]
    moved = (partner != index) & (slot % exp_dev == given)
    return jnp.where(moved, partner * exp_dev + swap_plan[partner, 1], slot)


def shards(tokens, route_ids, route_weights, swap_plan, gate_up, down):
    n_z = lax.axis_size("z")
    n_plane = lax.axis_size("y") * lax.axis_size("x")
    ep_size = n_z * n_plane
    rep = lax.axis_index("rep")
    core = rep % 2
    half = rep // 2
    exp_dev = gate_up.shape[0]
    experts = exp_dev * ep_size
    tok_dev, top_k = route_ids.shape
    routed = tok_dev * top_k
    capacity = max(2, (routed * 3 + 2 * experts - 1) // (2 * experts))
    places = experts * capacity
    width = tokens.shape[1]
    cut = [slice(i * width, (i + 1) * width) for i in range(4)]

    holder = holder_of(swap_plan, exp_dev)
    owners = holder[route_ids.reshape(routed)]
    catalog = jnp.arange(experts, dtype=jnp.int32)
    one_hot = (owners[:, None] == catalog[None, :]).astype(jnp.float32)
    earlier = (jnp.arange(routed)[:, None] > jnp.arange(routed)[None, :]).astype(jnp.float32)
    before = jnp.dot(earlier, one_hot, preferred_element_type=jnp.float32)
    position = jnp.sum(before * one_hot, axis=1).astype(jnp.int32)
    device = owners // exp_dev
    group = (device % n_plane) * n_z + device // n_plane
    place = (group * exp_dev + owners % exp_dev) * capacity + position
    hits = (place[:, None] == jnp.arange(places, dtype=jnp.int32)[None, :]).reshape(tok_dev, top_k, places)
    gather = jnp.sum(hits.astype(jnp.bfloat16), axis=1)
    mixing = jnp.sum(jnp.where(hits, route_weights[:, :, None], 0.0), axis=1)

    other = pair_swap(tokens, "rep", 1)
    low, high = pick(half == 0, tokens, other)
    features = jnp.concatenate([low, high], axis=1)
    outgoing = lax.dot_general(
        gather, features, (((0,), (0,)), ((), ())), preferred_element_type=jnp.float32
    ).astype(jnp.bfloat16)

    step = lax.all_to_all(
        outgoing.reshape(n_plane, places // n_plane, 2 * width), PLANE, 0, 0, tiled=True
    )
    step = step.reshape(n_plane, n_z, exp_dev, capacity, 2 * width).transpose(1, 2, 0, 3, 4)
    mine = lax.all_to_all(
        step.reshape(n_z, places // n_z, 2 * width), "z", 0, 0, tiled=True
    ).reshape(n_z, exp_dev, n_plane * capacity, 2 * width)

    theirs = pair_swap(mine, "rep", 0)
    even, odd = pick(core == 0, mine, theirs)

    results = []
    for index in range(exp_dev):
        first = even[:, index]
        second = odd[:, index]
        rows = jnp.concatenate(
            [first[..., : width], second[..., : width], first[..., width:], second[..., width:]], axis=-1
        )
        projected = jnp.einsum(
            "zrd,dgf->zrgf", rows, gate_up[index], preferred_element_type=jnp.float32
        )
        hidden = (jax.nn.silu(projected[:, :, 0]) * projected[:, :, 1]).astype(jnp.bfloat16)
        results.append(
            jnp.einsum(
                "zrf,fd->zrd", hidden, down[index], preferred_element_type=jnp.float32
            ).astype(jnp.bfloat16)
        )
    partial = jnp.stack(results, axis=1)

    part_even = jnp.concatenate([partial[..., cut[0]], partial[..., cut[2]]], axis=-1)
    part_odd = jnp.concatenate([partial[..., cut[1]], partial[..., cut[3]]], axis=-1)
    keep, send = pick(core == 0, part_even, part_odd)
    paired = (keep.astype(jnp.float32) + pair_swap(send, "rep", 0).astype(jnp.float32)).astype(
        jnp.bfloat16
    )

    back = lax.all_to_all(paired.reshape(n_z, places // n_z, 2 * width), "z", 0, 0, tiled=True)
    back = back.reshape(n_z, exp_dev, n_plane, capacity, 2 * width).transpose(2, 0, 1, 3, 4)
    returned = lax.all_to_all(
        back.reshape(n_plane, places // n_plane, 2 * width), PLANE, 0, 0, tiled=True
    )
    weighted = jnp.dot(
        mixing,
        returned.reshape(places, 2 * width).astype(jnp.float32),
        precision=lax.Precision.HIGHEST,
        preferred_element_type=jnp.float32,
    )
    own, away = pick(half == 0, weighted[:, :width], weighted[:, width:])
    return (own + pair_swap(away, "rep", 1)).astype(jnp.bfloat16)


def solution(mesh):
    rep_size, ep_size = mesh.devices.shape
    side = round(ep_size ** (1 / 3))
    grid = Mesh(np.asarray(mesh.devices).reshape(rep_size, side, side, side), ("rep",) + EP_AXES)
    return jax.shard_map(
        shards,
        mesh=grid,
        in_specs=(
            P(EP_AXES, "rep"),
            P(EP_AXES, None),
            P(EP_AXES, None),
            P(),
            P(EP_AXES, None, None, "rep"),
            P(EP_AXES, "rep", None),
        ),
        out_specs=P(EP_AXES, "rep"),
        check_vma=False,
    )
```

```python
import jax
import jax.numpy as jnp
import numpy as np
from jax import lax
from jax.sharding import Mesh
from jax.sharding import PartitionSpec as P

EP_AXES = ("z", "y", "x")
REP_AXES = ("zh", "core")
RING = ("zh", "z")
PLANE = ("y", "x")


def pair_swap(value, axis):
    return lax.ppermute(value, axis, [(0, 1), (1, 0)])


def ring_shift(value, shift):
    size = lax.axis_size(RING)
    return lax.ppermute(value, RING, [(i, (i + shift) % size) for i in range(size)])


def pick(flag, first, second):
    return jnp.where(flag, first, second), jnp.where(flag, second, first)


def holder_of(swap_plan, exp_dev):
    ep_size = swap_plan.shape[0]
    slot = jnp.arange(ep_size * exp_dev, dtype=jnp.int32)
    index = slot // exp_dev
    partner = swap_plan[index, 0]
    given = swap_plan[index, 1]
    moved = (partner != index) & (slot % exp_dev == given)
    return jnp.where(moved, partner * exp_dev + swap_plan[partner, 1], slot)


def shards(tokens, route_ids, route_weights, swap_plan, gate_up, down):
    n_z = lax.axis_size("z")
    n_plane = lax.axis_size("y") * lax.axis_size("x")
    ep_size = n_z * n_plane
    core = lax.axis_index("core")
    half = lax.axis_index("zh")
    exp_dev = gate_up.shape[0]
    experts = exp_dev * ep_size
    tok_dev, top_k = route_ids.shape
    routed = tok_dev * top_k
    capacity = max(2, (routed * 3 + 2 * experts - 1) // (2 * experts))
    places = experts * capacity
    width = tokens.shape[1]
    cut = [slice(i * width, (i + 1) * width) for i in range(4)]

    holder = holder_of(swap_plan, exp_dev)
    owners = holder[route_ids.reshape(routed)]
    catalog = jnp.arange(experts, dtype=jnp.int32)
    one_hot = (owners[:, None] == catalog[None, :]).astype(jnp.float32)
    earlier = (jnp.arange(routed)[:, None] > jnp.arange(routed)[None, :]).astype(jnp.float32)
    before = jnp.dot(earlier, one_hot, preferred_element_type=jnp.float32)
    position = jnp.sum(before * one_hot, axis=1).astype(jnp.int32)
    device = owners // exp_dev
    offset = (device // n_plane - lax.axis_index("z")) % n_z
    group = (device % n_plane) * n_z + offset
    place = (group * exp_dev + owners % exp_dev) * capacity + position
    hits = (place[:, None] == jnp.arange(places, dtype=jnp.int32)[None, :]).reshape(tok_dev, top_k, places)
    gather = jnp.sum(hits.astype(jnp.bfloat16), axis=1)
    mixing = jnp.sum(jnp.where(hits, route_weights[:, :, None], 0.0), axis=1)

    other = pair_swap(tokens, "zh")
    low, high = pick(half == 0, tokens, other)
    features = jnp.concatenate([low, high], axis=1)
    outgoing = lax.dot_general(
        gather, features, (((0,), (0,)), ((), ())), preferred_element_type=jnp.float32
    ).astype(jnp.bfloat16)

    step = lax.all_to_all(
        outgoing.reshape(n_plane, places // n_plane, 2 * width), PLANE, 0, 0, tiled=True
    )
    step = step.reshape(n_plane, n_z, exp_dev, capacity, 2 * width).transpose(1, 2, 0, 3, 4)
    step = step.reshape(n_z, exp_dev, n_plane * capacity, 2 * width)
    far = jnp.concatenate(
        [ring_shift(step[2, :1], 2), ring_shift(step[2, 1:], -2)], axis=0
    )
    mine = jnp.stack([step[0], ring_shift(step[1], 1), far, ring_shift(step[3], -1)])

    theirs = pair_swap(mine, "core")
    even, odd = pick(core == 0, mine, theirs)

    results = []
    for index in range(exp_dev):
        first = even[:, index]
        second = odd[:, index]
        rows = jnp.concatenate(
            [first[..., : width], second[..., : width], first[..., width:], second[..., width:]], axis=-1
        )
        projected = jnp.einsum(
            "zrd,dgf->zrgf", rows, gate_up[index], preferred_element_type=jnp.float32
        )
        hidden = (jax.nn.silu(projected[:, :, 0]) * projected[:, :, 1]).astype(jnp.bfloat16)
        results.append(
            jnp.einsum(
                "zrf,fd->zrd", hidden, down[index], preferred_element_type=jnp.float32
            ).astype(jnp.bfloat16)
        )
    partial = jnp.stack(results, axis=1)

    part_even = jnp.concatenate([partial[..., cut[0]], partial[..., cut[2]]], axis=-1)
    part_odd = jnp.concatenate([partial[..., cut[1]], partial[..., cut[3]]], axis=-1)
    keep, send = pick(core == 0, part_even, part_odd)
    paired = (keep.astype(jnp.float32) + pair_swap(send, "core").astype(jnp.float32)).astype(
        jnp.bfloat16
    )

    far = jnp.concatenate(
        [ring_shift(paired[2, :1], -2), ring_shift(paired[2, 1:], 2)], axis=0
    )
    back = jnp.stack([paired[0], ring_shift(paired[1], -1), far, ring_shift(paired[3], 1)])
    back = back.reshape(n_z, exp_dev, n_plane, capacity, 2 * width).transpose(2, 0, 1, 3, 4)
    returned = lax.all_to_all(
        back.reshape(n_plane, places // n_plane, 2 * width), PLANE, 0, 0, tiled=True
    )
    weighted = jnp.dot(
        mixing,
        returned.reshape(places, 2 * width).astype(jnp.float32),
        precision=lax.Precision.HIGHEST,
        preferred_element_type=jnp.float32,
    )
    own, away = pick(half == 0, weighted[:, :width], weighted[:, width:])
    return (own + pair_swap(away, "zh")).astype(jnp.bfloat16)


def solution(mesh):
    rep_size, ep_size = mesh.devices.shape
    side = round(ep_size ** (1 / 3))
    shape = (2, rep_size // 2, side, side, side)
    grid = Mesh(np.asarray(mesh.devices).reshape(shape), REP_AXES + EP_AXES)
    return jax.shard_map(
        shards,
        mesh=grid,
        in_specs=(
            P(EP_AXES, REP_AXES),
            P(EP_AXES, None),
            P(EP_AXES, None),
            P(),
            P(EP_AXES, None, None, REP_AXES),
            P(EP_AXES, REP_AXES, None),
        ),
        out_specs=P(EP_AXES, REP_AXES),
        check_vma=False,
    )
```

```python
import jax
import jax.numpy as jnp
import numpy as np
from jax import lax
from jax.sharding import Mesh
from jax.sharding import PartitionSpec as P

EP_AXES = ("z", "y", "x")
REP_AXES = ("zh", "core")
RING = ("zh", "z")
PLANE = ("y", "x")


def pair_swap(value, axis):
    return lax.ppermute(value, axis, [(0, 1), (1, 0)])


def ring_shift(value, shift):
    size = lax.axis_size(RING)
    return lax.ppermute(value, RING, [(i, (i + shift) % size) for i in range(size)])


def plane_a2a(value):
    return lax.all_to_all(value, PLANE, 0, 0, tiled=True)


def ring_out(chunks):
    cut = chunks.shape[1] // 2
    far = jnp.concatenate([ring_shift(chunks[2, :cut], 2), ring_shift(chunks[2, cut:], -2)])
    return jnp.stack([chunks[0], ring_shift(chunks[1], 1), far, ring_shift(chunks[3], -1)])


def ring_back(chunks):
    cut = chunks.shape[1] // 2
    far = jnp.concatenate([ring_shift(chunks[2, :cut], -2), ring_shift(chunks[2, cut:], 2)])
    return jnp.stack([chunks[0], ring_shift(chunks[1], -1), far, ring_shift(chunks[3], 1)])


def pick(flag, first, second):
    return jnp.where(flag, first, second), jnp.where(flag, second, first)


def holder_of(swap_plan, exp_dev):
    ep_size = swap_plan.shape[0]
    slot = jnp.arange(ep_size * exp_dev, dtype=jnp.int32)
    index = slot // exp_dev
    partner = swap_plan[index, 0]
    given = swap_plan[index, 1]
    moved = (partner != index) & (slot % exp_dev == given)
    return jnp.where(moved, partner * exp_dev + swap_plan[partner, 1], slot)


def shards(tokens, route_ids, route_weights, swap_plan, gate_up, down):
    n_z = lax.axis_size("z")
    n_plane = lax.axis_size("y") * lax.axis_size("x")
    ep_size = n_z * n_plane
    core = lax.axis_index("core")
    half = lax.axis_index("zh")
    exp_dev = gate_up.shape[0]
    experts = exp_dev * ep_size
    tok_dev, top_k = route_ids.shape
    routed = tok_dev * top_k
    capacity = max(2, (routed * 3 + 2 * experts - 1) // (2 * experts))
    places = experts * capacity
    width = tokens.shape[1]
    cut = [slice(i * width, (i + 1) * width) for i in range(4)]

    holder = holder_of(swap_plan, exp_dev)
    owners = holder[route_ids.reshape(routed)]
    catalog = jnp.arange(experts, dtype=jnp.int32)
    one_hot = (owners[:, None] == catalog[None, :]).astype(jnp.float32)
    earlier = (jnp.arange(routed)[:, None] > jnp.arange(routed)[None, :]).astype(jnp.float32)
    before = jnp.dot(earlier, one_hot, preferred_element_type=jnp.float32)
    position = jnp.sum(before * one_hot, axis=1).astype(jnp.int32)
    device = owners // exp_dev
    plane = device % n_plane
    offset = (device // n_plane - lax.axis_index("z")) % n_z
    slot = owners % exp_dev
    rank = jnp.where(slot == 0, plane * n_z + offset, offset * n_plane + plane)
    place = (slot * n_z * n_plane + rank) * capacity + position
    hits = (place[:, None] == jnp.arange(places, dtype=jnp.int32)[None, :]).reshape(tok_dev, top_k, places)
    gather = jnp.sum(hits.astype(jnp.bfloat16), axis=1)
    mixing = jnp.sum(jnp.where(hits, route_weights[:, :, None], 0.0), axis=1)

    other = pair_swap(tokens, "zh")
    low, high = pick(half == 0, tokens, other)
    features = jnp.concatenate([low, high], axis=1)
    outgoing = lax.dot_general(
        gather, features, (((0,), (0,)), ((), ())), preferred_element_type=jnp.float32
    ).astype(jnp.bfloat16)

    half_rows = places // exp_dev
    wide = 2 * width
    first = outgoing[:half_rows].reshape(n_plane, half_rows // n_plane, wide)
    second = outgoing[half_rows:].reshape(n_z, half_rows // n_z, wide)
    first = plane_a2a(first)
    second = ring_out(second)
    first = first.reshape(n_plane, n_z, capacity, wide).transpose(1, 0, 2, 3)
    second = second.reshape(n_z, n_plane, capacity, wide).transpose(1, 0, 2, 3)
    first = ring_out(first.reshape(n_z, half_rows // n_z, wide))
    second = plane_a2a(second.reshape(n_plane, half_rows // n_plane, wide))
    arrived = [first.reshape(half_rows, wide), second.reshape(half_rows, wide)]

    paired = []
    for index in range(exp_dev):
        mine = arrived[index]
        theirs = pair_swap(mine, "core")
        even, odd = pick(core == 0, mine, theirs)
        rows = jnp.concatenate(
            [even[:, :width], odd[:, :width], even[:, width:], odd[:, width:]], axis=-1
        )
        projected = jnp.einsum(
            "rd,dgf->rgf", rows, gate_up[index], preferred_element_type=jnp.float32
        )
        hidden = (jax.nn.silu(projected[:, 0]) * projected[:, 1]).astype(jnp.bfloat16)
        partial = jnp.dot(hidden, down[index], preferred_element_type=jnp.float32).astype(jnp.bfloat16)
        part_even = jnp.concatenate([partial[:, cut[0]], partial[:, cut[2]]], axis=-1)
        part_odd = jnp.concatenate([partial[:, cut[1]], partial[:, cut[3]]], axis=-1)
        keep, send = pick(core == 0, part_even, part_odd)
        paired.append(
            (keep.astype(jnp.float32) + pair_swap(send, "core").astype(jnp.float32)).astype(jnp.bfloat16)
        )

    first = ring_back(paired[0].reshape(n_z, half_rows // n_z, wide))
    second = plane_a2a(paired[1].reshape(n_plane, half_rows // n_plane, wide))
    first = first.reshape(n_z, n_plane, capacity, wide).transpose(1, 0, 2, 3)
    second = second.reshape(n_plane, n_z, capacity, wide).transpose(1, 0, 2, 3)
    first = plane_a2a(first.reshape(n_plane, half_rows // n_plane, wide))
    second = ring_back(second.reshape(n_z, half_rows // n_z, wide))
    returned = jnp.concatenate([first.reshape(half_rows, wide), second.reshape(half_rows, wide)])
    weighted = jnp.dot(
        mixing,
        returned.astype(jnp.float32),
        precision=lax.Precision.HIGHEST,
        preferred_element_type=jnp.float32,
    )
    own, away = pick(half == 0, weighted[:, :width], weighted[:, width:])
    return (own + pair_swap(away, "zh")).astype(jnp.bfloat16)


def solution(mesh):
    rep_size, ep_size = mesh.devices.shape
    side = round(ep_size ** (1 / 3))
    shape = (2, rep_size // 2, side, side, side)
    grid = Mesh(np.asarray(mesh.devices).reshape(shape), REP_AXES + EP_AXES)
    return jax.shard_map(
        shards,
        mesh=grid,
        in_specs=(
            P(EP_AXES, REP_AXES),
            P(EP_AXES, None),
            P(EP_AXES, None),
            P(),
            P(EP_AXES, None, None, REP_AXES),
            P(EP_AXES, REP_AXES, None),
        ),
        out_specs=P(EP_AXES, REP_AXES),
        check_vma=False,
    )
```

```python
import jax
import jax.numpy as jnp
import numpy as np
from jax import lax
from jax.sharding import Mesh
from jax.sharding import PartitionSpec as P

EP_AXES = ("z", "y", "x")
REP_AXES = ("zh", "core")
RING = ("zh", "z")
PLANE = ("y", "x")


def pair_swap(value, axis):
    return lax.ppermute(value, axis, [(0, 1), (1, 0)])


def ring_shift(value, shift):
    size = lax.axis_size(RING)
    return lax.ppermute(value, RING, [(i, (i + shift) % size) for i in range(size)])


def plane_a2a(value):
    return lax.all_to_all(value, PLANE, 0, 0, tiled=True)


def ring_out(chunks):
    cut = chunks.shape[1] // 2
    far = jnp.concatenate([ring_shift(chunks[2, :cut], 2), ring_shift(chunks[2, cut:], -2)])
    return jnp.stack([chunks[0], ring_shift(chunks[1], 1), far, ring_shift(chunks[3], -1)])


def ring_back(chunks):
    cut = chunks.shape[1] // 2
    far = jnp.concatenate([ring_shift(chunks[2, :cut], -2), ring_shift(chunks[2, cut:], 2)])
    return jnp.stack([chunks[0], ring_shift(chunks[1], -1), far, ring_shift(chunks[3], 1)])


def pick(flag, first, second):
    return jnp.where(flag, first, second), jnp.where(flag, second, first)


def holder_of(swap_plan, exp_dev):
    ep_size = swap_plan.shape[0]
    slot = jnp.arange(ep_size * exp_dev, dtype=jnp.int32)
    partner = jnp.repeat(swap_plan[:, 0], exp_dev)
    given = jnp.repeat(swap_plan[:, 1], exp_dev)
    choose = (partner[:, None] == jnp.arange(ep_size, dtype=jnp.int32)[None, :]).astype(jnp.float32)
    partner_given = jnp.dot(choose, swap_plan[:, 1].astype(jnp.float32)).astype(jnp.int32)
    moved = (partner != slot // exp_dev) & (slot % exp_dev == given)
    return jnp.where(moved, partner * exp_dev + partner_given, slot)


def shards(tokens, route_ids, route_weights, swap_plan, gate_up, down):
    n_z = lax.axis_size("z")
    n_plane = lax.axis_size("y") * lax.axis_size("x")
    ep_size = n_z * n_plane
    core = lax.axis_index("core")
    half = lax.axis_index("zh")
    exp_dev = gate_up.shape[0]
    experts = exp_dev * ep_size
    tok_dev, top_k = route_ids.shape
    routed = tok_dev * top_k
    capacity = max(2, (routed * 3 + 2 * experts - 1) // (2 * experts))
    places = experts * capacity
    width = tokens.shape[1]
    cut = [slice(i * width, (i + 1) * width) for i in range(4)]

    holder = holder_of(swap_plan, exp_dev)
    catalog = jnp.arange(experts, dtype=jnp.int32)
    named = (route_ids.reshape(routed)[:, None] == catalog[None, :]).astype(jnp.float32)
    owners = jnp.dot(named, holder.astype(jnp.float32)).astype(jnp.int32)
    one_hot = (owners[:, None] == catalog[None, :]).astype(jnp.float32)
    earlier = (jnp.arange(routed)[:, None] > jnp.arange(routed)[None, :]).astype(jnp.float32)
    before = jnp.dot(earlier, one_hot, preferred_element_type=jnp.float32)
    position = jnp.sum(before * one_hot, axis=1).astype(jnp.int32)
    device = owners // exp_dev
    plane = device % n_plane
    offset = (device // n_plane - lax.axis_index("z")) % n_z
    slot = owners % exp_dev
    rank = jnp.where(slot == 0, plane * n_z + offset, offset * n_plane + plane)
    place = (slot * n_z * n_plane + rank) * capacity + position
    hits = (place[:, None] == jnp.arange(places, dtype=jnp.int32)[None, :]).reshape(tok_dev, top_k, places)
    gather = jnp.sum(hits.astype(jnp.bfloat16), axis=1)
    mixing = jnp.sum(jnp.where(hits, route_weights[:, :, None], 0.0), axis=1)

    other = pair_swap(tokens, "zh")
    low, high = pick(half == 0, tokens, other)
    features = jnp.concatenate([low, high], axis=1)
    outgoing = lax.dot_general(
        gather, features, (((0,), (0,)), ((), ())), preferred_element_type=jnp.float32
    ).astype(jnp.bfloat16)

    half_rows = places // exp_dev
    wide = 2 * width
    first = outgoing[:half_rows].reshape(n_plane, half_rows // n_plane, wide)
    second = outgoing[half_rows:].reshape(n_z, half_rows // n_z, wide)
    first = plane_a2a(first)
    second = ring_out(second)
    first = first.reshape(n_plane, n_z, capacity, wide).transpose(1, 0, 2, 3)
    second = second.reshape(n_z, n_plane, capacity, wide).transpose(1, 0, 2, 3)
    first = ring_out(first.reshape(n_z, half_rows // n_z, wide))
    second = plane_a2a(second.reshape(n_plane, half_rows // n_plane, wide))
    arrived = [first.reshape(half_rows, wide), second.reshape(half_rows, wide)]

    rows = []
    for mine in arrived:
        theirs = pair_swap(mine, "core")
        even, odd = pick(core == 0, mine, theirs)
        rows.append(
            jnp.concatenate([even[:, :width], odd[:, :width], even[:, width:], odd[:, width:]], axis=-1)
        )
    projected = jnp.einsum(
        "srd,sdgf->srgf", jnp.stack(rows), gate_up, preferred_element_type=jnp.float32
    )
    hidden = (jax.nn.silu(projected[:, :, 0]) * projected[:, :, 1]).astype(jnp.bfloat16)
    partial = jnp.einsum("srf,sfd->srd", hidden, down, preferred_element_type=jnp.float32).astype(
        jnp.bfloat16
    )
    part_even = jnp.concatenate([partial[..., cut[0]], partial[..., cut[2]]], axis=-1)
    part_odd = jnp.concatenate([partial[..., cut[1]], partial[..., cut[3]]], axis=-1)
    keep, send = pick(core == 0, part_even, part_odd)
    paired = (keep.astype(jnp.float32) + pair_swap(send, "core").astype(jnp.float32)).astype(jnp.bfloat16)

    first = ring_back(paired[0].reshape(n_z, half_rows // n_z, wide))
    second = plane_a2a(paired[1].reshape(n_plane, half_rows // n_plane, wide))
    first = first.reshape(n_z, n_plane, capacity, wide).transpose(1, 0, 2, 3)
    second = second.reshape(n_plane, n_z, capacity, wide).transpose(1, 0, 2, 3)
    first = plane_a2a(first.reshape(n_plane, half_rows // n_plane, wide))
    second = ring_back(second.reshape(n_z, half_rows // n_z, wide))
    returned = jnp.concatenate([first.reshape(half_rows, wide), second.reshape(half_rows, wide)])
    weighted = jnp.dot(
        mixing,
        returned.astype(jnp.float32),
        precision=lax.Precision.HIGHEST,
        preferred_element_type=jnp.float32,
    )
    own, away = pick(half == 0, weighted[:, :width], weighted[:, width:])
    return (own + pair_swap(away, "zh")).astype(jnp.bfloat16)


def solution(mesh):
    rep_size, ep_size = mesh.devices.shape
    side = round(ep_size ** (1 / 3))
    shape = (2, rep_size // 2, side, side, side)
    grid = Mesh(np.asarray(mesh.devices).reshape(shape), REP_AXES + EP_AXES)
    return jax.shard_map(
        shards,
        mesh=grid,
        in_specs=(
            P(EP_AXES, REP_AXES),
            P(EP_AXES, None),
            P(EP_AXES, None),
            P(),
            P(EP_AXES, None, None, REP_AXES),
            P(EP_AXES, REP_AXES, None),
        ),
        out_specs=P(EP_AXES, REP_AXES),
        check_vma=False,
    )
```

```python
import jax
import jax.numpy as jnp
import numpy as np
from jax import lax
from jax.sharding import Mesh
from jax.sharding import PartitionSpec as P

EP_AXES = ("z", "y", "x")
REP_AXES = ("zh", "core")
RING = ("zh", "z")
PLANE = ("y", "x")


def pair_swap(value, axis):
    return lax.ppermute(value, axis, [(0, 1), (1, 0)])


def ring_shift(value, shift):
    size = lax.axis_size(RING)
    return lax.ppermute(value, RING, [(i, (i + shift) % size) for i in range(size)])


def plane_a2a(value):
    return lax.all_to_all(value, PLANE, 0, 0, tiled=True)


def ring_out(chunks):
    cut = chunks.shape[1] // 2
    far = jnp.concatenate([ring_shift(chunks[2, :cut], 2), ring_shift(chunks[2, cut:], -2)])
    return jnp.stack([chunks[0], ring_shift(chunks[1], 1), far, ring_shift(chunks[3], -1)])


def ring_back(chunks):
    cut = chunks.shape[1] // 2
    far = jnp.concatenate([ring_shift(chunks[2, :cut], -2), ring_shift(chunks[2, cut:], 2)])
    return jnp.stack([chunks[0], ring_shift(chunks[1], -1), far, ring_shift(chunks[3], 1)])


def pick(flag, first, second):
    return jnp.where(flag, first, second), jnp.where(flag, second, first)


def holder_of(swap_plan, exp_dev):
    ep_size = swap_plan.shape[0]
    slot = jnp.arange(ep_size * exp_dev, dtype=jnp.int32)
    partner = jnp.repeat(swap_plan[:, 0], exp_dev)
    given = jnp.repeat(swap_plan[:, 1], exp_dev)
    choose = (partner[:, None] == jnp.arange(ep_size, dtype=jnp.int32)[None, :]).astype(jnp.float32)
    partner_given = jnp.dot(choose, swap_plan[:, 1].astype(jnp.float32)).astype(jnp.int32)
    moved = (partner != slot // exp_dev) & (slot % exp_dev == given)
    return jnp.where(moved, partner * exp_dev + partner_given, slot)


def shards(tokens, route_ids, route_weights, swap_plan, gate_up, down):
    n_z = lax.axis_size("z")
    n_plane = lax.axis_size("y") * lax.axis_size("x")
    ep_size = n_z * n_plane
    core = lax.axis_index("core")
    half = lax.axis_index("zh")
    exp_dev = gate_up.shape[0]
    experts = exp_dev * ep_size
    tok_dev, top_k = route_ids.shape
    routed = tok_dev * top_k
    capacity = max(2, (routed * 3 + 2 * experts - 1) // (2 * experts))
    places = experts * capacity
    width = tokens.shape[1]
    cut = [slice(i * width, (i + 1) * width) for i in range(4)]

    holder = holder_of(swap_plan, exp_dev)
    catalog = jnp.arange(experts, dtype=jnp.int32)
    named = (route_ids.reshape(routed)[:, None] == catalog[None, :]).astype(jnp.float32)
    owners = jnp.dot(named, holder.astype(jnp.float32)).astype(jnp.int32)
    one_hot = (owners[:, None] == catalog[None, :]).astype(jnp.float32)
    earlier = (jnp.arange(routed)[:, None] > jnp.arange(routed)[None, :]).astype(jnp.float32)
    before = jnp.dot(earlier, one_hot, preferred_element_type=jnp.float32)
    position = jnp.sum(before * one_hot, axis=1).astype(jnp.int32)
    device = owners // exp_dev
    plane = device % n_plane
    offset = (device // n_plane - lax.axis_index("z")) % n_z
    slot = owners % exp_dev
    rank = jnp.where(slot == 0, plane * n_z + offset, offset * n_plane + plane)
    place = (slot * n_z * n_plane + rank) * capacity + position
    hits = (place[:, None] == jnp.arange(places, dtype=jnp.int32)[None, :]).reshape(tok_dev, top_k, places)
    gather = jnp.sum(hits.astype(jnp.bfloat16), axis=1)
    mixing = jnp.sum(jnp.where(hits, route_weights[:, :, None], 0.0), axis=1)

    other = pair_swap(tokens, "zh")
    low, high = pick(half == 0, tokens, other)
    features = jnp.concatenate([low, high], axis=1)
    outgoing = lax.dot_general(
        gather, features, (((0,), (0,)), ((), ())), preferred_element_type=jnp.float32
    ).astype(jnp.bfloat16)

    half_rows = places // exp_dev
    wide = 2 * width
    first = outgoing[:half_rows].reshape(n_plane, half_rows // n_plane, wide)
    second = outgoing[half_rows:].reshape(n_z, half_rows // n_z, wide)
    first = plane_a2a(first)
    second = ring_out(second)
    first = first.reshape(n_plane, n_z, capacity, wide).transpose(1, 0, 2, 3)
    second = second.reshape(n_z, n_plane, capacity, wide).transpose(1, 0, 2, 3)
    first = ring_out(first.reshape(n_z, half_rows // n_z, wide))
    second = plane_a2a(second.reshape(n_plane, half_rows // n_plane, wide))
    arrived = [first.reshape(half_rows, wide), second.reshape(half_rows, wide)]

    rows = []
    for mine in arrived:
        theirs = pair_swap(mine, "core")
        even, odd = pick(core == 0, mine, theirs)
        rows.append(
            jnp.concatenate([even[:, :width], odd[:, :width], even[:, width:], odd[:, width:]], axis=-1)
        )
    projected = jnp.einsum(
        "srd,sdgf->srgf", jnp.stack(rows), gate_up, preferred_element_type=jnp.float32
    )
    hidden = (jax.nn.silu(projected[:, :, 0]) * projected[:, :, 1]).astype(jnp.bfloat16)
    partial = jnp.einsum("srf,sfd->srd", hidden, down, preferred_element_type=jnp.float32).astype(
        jnp.bfloat16
    )
    part_even = jnp.concatenate([partial[..., cut[0]], partial[..., cut[2]]], axis=-1)
    part_odd = jnp.concatenate([partial[..., cut[1]], partial[..., cut[3]]], axis=-1)
    keep, send = pick(core == 0, part_even, part_odd)
    paired = (keep.astype(jnp.float32) + pair_swap(send, "core").astype(jnp.float32)).astype(jnp.bfloat16)

    first = ring_back(paired[0].reshape(n_z, half_rows // n_z, wide))
    second = plane_a2a(paired[1].reshape(n_plane, half_rows // n_plane, wide))
    first = first.reshape(n_z, n_plane, capacity, wide).transpose(1, 0, 2, 3)
    second = second.reshape(n_plane, n_z, capacity, wide).transpose(1, 0, 2, 3)
    first = plane_a2a(first.reshape(n_plane, half_rows // n_plane, wide))
    second = ring_back(second.reshape(n_z, half_rows // n_z, wide))
    returned = jnp.concatenate([first.reshape(half_rows, wide), second.reshape(half_rows, wide)])
    weighted = jnp.dot(
        mixing,
        returned.astype(jnp.float32),
        precision=lax.Precision.HIGHEST,
        preferred_element_type=jnp.float32,
    )
    own, away = pick(half == 0, weighted[:, :width], weighted[:, width:])
    return (own + pair_swap(away.astype(jnp.bfloat16), "zh").astype(jnp.float32)).astype(jnp.bfloat16)


def solution(mesh):
    rep_size, ep_size = mesh.devices.shape
    side = round(ep_size ** (1 / 3))
    shape = (2, rep_size // 2, side, side, side)
    grid = Mesh(np.asarray(mesh.devices).reshape(shape), REP_AXES + EP_AXES)
    return jax.shard_map(
        shards,
        mesh=grid,
        in_specs=(
            P(EP_AXES, REP_AXES),
            P(EP_AXES, None),
            P(EP_AXES, None),
            P(),
            P(EP_AXES, None, None, REP_AXES),
            P(EP_AXES, REP_AXES, None),
        ),
        out_specs=P(EP_AXES, REP_AXES),
        check_vma=False,
    )
```

```python
import jax
import jax.numpy as jnp
import numpy as np
from jax import lax
from jax.sharding import Mesh
from jax.sharding import PartitionSpec as P

EP_AXES = ("z", "y", "x")
REP_AXES = ("zh", "core")
RING = ("zh", "z")
PLANE = ("y", "x")


def pair_swap(value, axis):
    return lax.ppermute(value, axis, [(0, 1), (1, 0)])


def ring_shift(value, shift):
    size = lax.axis_size(RING)
    return lax.ppermute(value, RING, [(i, (i + shift) % size) for i in range(size)])


def plane_a2a(value):
    return lax.all_to_all(value, PLANE, 0, 0, tiled=True)


def ring_out(chunks):
    cut = chunks.shape[1] // 2
    far = jnp.concatenate([ring_shift(chunks[2, :cut], 2), ring_shift(chunks[2, cut:], -2)])
    return jnp.stack([chunks[0], ring_shift(chunks[1], 1), far, ring_shift(chunks[3], -1)])


def ring_back(chunks):
    cut = chunks.shape[1] // 2
    far = jnp.concatenate([ring_shift(chunks[2, :cut], -2), ring_shift(chunks[2, cut:], 2)])
    return jnp.stack([chunks[0], ring_shift(chunks[1], -1), far, ring_shift(chunks[3], 1)])


def pick(flag, first, second):
    return jnp.where(flag, first, second), jnp.where(flag, second, first)


def holder_of(swap_plan, exp_dev):
    ep_size = swap_plan.shape[0]
    slot = jnp.arange(ep_size * exp_dev, dtype=jnp.int32)
    partner = jnp.repeat(swap_plan[:, 0], exp_dev)
    given = jnp.repeat(swap_plan[:, 1], exp_dev)
    choose = (partner[:, None] == jnp.arange(ep_size, dtype=jnp.int32)[None, :]).astype(jnp.float32)
    partner_given = jnp.dot(choose, swap_plan[:, 1].astype(jnp.float32)).astype(jnp.int32)
    moved = (partner != slot // exp_dev) & (slot % exp_dev == given)
    return jnp.where(moved, partner * exp_dev + partner_given, slot)


def shards(tokens, route_ids, route_weights, swap_plan, gate_up, down):
    n_z = lax.axis_size("z")
    n_plane = lax.axis_size("y") * lax.axis_size("x")
    ep_size = n_z * n_plane
    core = lax.axis_index("core")
    half = lax.axis_index("zh")
    exp_dev = gate_up.shape[0]
    experts = exp_dev * ep_size
    tok_dev, top_k = route_ids.shape
    routed = tok_dev * top_k
    capacity = max(2, (routed * 3 + 2 * experts - 1) // (2 * experts))
    places = experts * capacity
    width = tokens.shape[1]
    cut = [slice(i * width, (i + 1) * width) for i in range(4)]

    holder = holder_of(swap_plan, exp_dev)
    catalog = jnp.arange(experts, dtype=jnp.int32)
    named = (route_ids.reshape(routed)[:, None] == catalog[None, :]).astype(jnp.float32)
    owners = jnp.dot(named, holder.astype(jnp.float32)).astype(jnp.int32)
    one_hot = (owners[:, None] == catalog[None, :]).astype(jnp.float32)
    earlier = (jnp.arange(routed)[:, None] > jnp.arange(routed)[None, :]).astype(jnp.float32)
    before = jnp.dot(earlier, one_hot, preferred_element_type=jnp.float32)
    position = jnp.sum(before * one_hot, axis=1).astype(jnp.int32)
    device = owners // exp_dev
    plane = device % n_plane
    offset = (device // n_plane - lax.axis_index("z")) % n_z
    slot = owners % exp_dev
    rank = jnp.where(slot == 0, plane * n_z + offset, offset * n_plane + plane)
    place = (slot * n_z * n_plane + rank) * capacity + position
    hits = (place[:, None] == jnp.arange(places, dtype=jnp.int32)[None, :]).reshape(tok_dev, top_k, places)
    gather = jnp.sum(hits.astype(jnp.bfloat16), axis=1)
    mixing = jnp.sum(jnp.where(hits, route_weights[:, :, None], 0.0), axis=1)

    other = pair_swap(tokens, "zh")
    low, high = pick(half == 0, tokens, other)
    features = jnp.concatenate([low, high], axis=1)
    outgoing = lax.dot_general(
        gather, features, (((0,), (0,)), ((), ())), preferred_element_type=jnp.float32
    ).astype(jnp.bfloat16)

    half_rows = places // exp_dev
    wide = 2 * width
    first = outgoing[:half_rows].reshape(n_plane, half_rows // n_plane, wide)
    second = outgoing[half_rows:].reshape(n_z, half_rows // n_z, wide)
    first = plane_a2a(first)
    second = ring_out(second)
    first = first.reshape(n_plane, n_z, capacity, wide).transpose(1, 0, 2, 3)
    second = second.reshape(n_z, n_plane, capacity, wide).transpose(1, 0, 2, 3)
    first = ring_out(first.reshape(n_z, half_rows // n_z, wide))
    second = plane_a2a(second.reshape(n_plane, half_rows // n_plane, wide))
    arrived = [first.reshape(half_rows, wide), second.reshape(half_rows, wide)]

    paired = []
    for index, mine in enumerate(arrived):
        theirs = pair_swap(mine, "core")
        even, odd = pick(core == 0, mine, theirs)
        rows = jnp.concatenate([even[:, :width], odd[:, :width], even[:, width:], odd[:, width:]], axis=-1)
        projected = jnp.einsum("rd,sdgf->srgf", rows, gate_up, preferred_element_type=jnp.float32)[index]
        hidden = (jax.nn.silu(projected[:, 0]) * projected[:, 1]).astype(jnp.bfloat16)
        partial = jnp.dot(hidden, down[index], preferred_element_type=jnp.float32).astype(jnp.bfloat16)
        part_even = jnp.concatenate([partial[:, cut[0]], partial[:, cut[2]]], axis=-1)
        part_odd = jnp.concatenate([partial[:, cut[1]], partial[:, cut[3]]], axis=-1)
        keep, send = pick(core == 0, part_even, part_odd)
        paired.append(
            (keep.astype(jnp.float32) + pair_swap(send, "core").astype(jnp.float32)).astype(jnp.bfloat16)
        )

    first = ring_back(paired[0].reshape(n_z, half_rows // n_z, wide))
    second = plane_a2a(paired[1].reshape(n_plane, half_rows // n_plane, wide))
    first = first.reshape(n_z, n_plane, capacity, wide).transpose(1, 0, 2, 3)
    second = second.reshape(n_plane, n_z, capacity, wide).transpose(1, 0, 2, 3)
    first = plane_a2a(first.reshape(n_plane, half_rows // n_plane, wide))
    second = ring_back(second.reshape(n_z, half_rows // n_z, wide))
    returned = jnp.concatenate([first.reshape(half_rows, wide), second.reshape(half_rows, wide)])
    weighted = jnp.dot(
        mixing,
        returned.astype(jnp.float32),
        precision=lax.Precision.HIGHEST,
        preferred_element_type=jnp.float32,
    )
    own, away = pick(half == 0, weighted[:, :width], weighted[:, width:])
    return (own + pair_swap(away.astype(jnp.bfloat16), "zh").astype(jnp.float32)).astype(jnp.bfloat16)


def solution(mesh):
    rep_size, ep_size = mesh.devices.shape
    side = round(ep_size ** (1 / 3))
    shape = (2, rep_size // 2, side, side, side)
    grid = Mesh(np.asarray(mesh.devices).reshape(shape), REP_AXES + EP_AXES)
    return jax.shard_map(
        shards,
        mesh=grid,
        in_specs=(
            P(EP_AXES, REP_AXES),
            P(EP_AXES, None),
            P(EP_AXES, None),
            P(),
            P(EP_AXES, None, None, REP_AXES),
            P(EP_AXES, REP_AXES, None),
        ),
        out_specs=P(EP_AXES, REP_AXES),
        check_vma=False,
    )
```

```python
import jax
import jax.numpy as jnp
import numpy as np
from jax import lax
from jax.sharding import Mesh
from jax.sharding import PartitionSpec as P

EP_AXES = ("z", "y", "x")
REP_AXES = ("zh", "core")
RING = ("zh", "z")
PLANE = ("y", "x")


def pair_swap(value, axis):
    return lax.ppermute(value, axis, [(0, 1), (1, 0)])


def ring_shift(value, shift):
    size = lax.axis_size(RING)
    return lax.ppermute(value, RING, [(i, (i + shift) % size) for i in range(size)])


def plane_a2a(value):
    return lax.all_to_all(value, PLANE, 0, 0, tiled=True)


def ring_out(chunks):
    cut = chunks.shape[1] // 2
    far = jnp.concatenate([ring_shift(chunks[2, :cut], 2), ring_shift(chunks[2, cut:], -2)])
    return jnp.stack([chunks[0], ring_shift(chunks[1], 1), far, ring_shift(chunks[3], -1)])


def ring_back(chunks):
    cut = chunks.shape[1] // 2
    far = jnp.concatenate([ring_shift(chunks[2, :cut], -2), ring_shift(chunks[2, cut:], 2)])
    return jnp.stack([chunks[0], ring_shift(chunks[1], -1), far, ring_shift(chunks[3], 1)])


def pick(flag, first, second):
    return jnp.where(flag, first, second), jnp.where(flag, second, first)


def holder_of(swap_plan, exp_dev):
    ep_size = swap_plan.shape[0]
    slot = jnp.arange(ep_size * exp_dev, dtype=jnp.int32)
    partner = jnp.repeat(swap_plan[:, 0], exp_dev)
    given = jnp.repeat(swap_plan[:, 1], exp_dev)
    choose = (partner[:, None] == jnp.arange(ep_size, dtype=jnp.int32)[None, :]).astype(jnp.float32)
    partner_given = jnp.dot(choose, swap_plan[:, 1].astype(jnp.float32)).astype(jnp.int32)
    moved = (partner != slot // exp_dev) & (slot % exp_dev == given)
    return jnp.where(moved, partner * exp_dev + partner_given, slot)


def shards(tokens, route_ids, route_weights, swap_plan, gate_up, down):
    n_z = lax.axis_size("z")
    n_plane = lax.axis_size("y") * lax.axis_size("x")
    ep_size = n_z * n_plane
    core = lax.axis_index("core")
    half = lax.axis_index("zh")
    exp_dev = gate_up.shape[0]
    experts = exp_dev * ep_size
    tok_dev, top_k = route_ids.shape
    routed = tok_dev * top_k
    capacity = max(2, (routed * 3 + 2 * experts - 1) // (2 * experts))
    places = experts * capacity
    width = tokens.shape[1]
    cut = [slice(i * width, (i + 1) * width) for i in range(4)]

    holder = holder_of(swap_plan, exp_dev)
    catalog = jnp.arange(experts, dtype=jnp.int32)
    named = (route_ids.reshape(routed)[:, None] == catalog[None, :]).astype(jnp.float32)
    owners = jnp.dot(named, holder.astype(jnp.float32)).astype(jnp.int32)
    one_hot = (owners[:, None] == catalog[None, :]).astype(jnp.float32)
    earlier = (jnp.arange(routed)[:, None] > jnp.arange(routed)[None, :]).astype(jnp.float32)
    before = jnp.dot(earlier, one_hot, preferred_element_type=jnp.float32)
    position = jnp.sum(before * one_hot, axis=1).astype(jnp.int32)
    device = owners // exp_dev
    plane = device % n_plane
    offset = (device // n_plane - lax.axis_index("z")) % n_z
    slot = owners % exp_dev
    rank = jnp.where(slot == 0, plane * n_z + offset, offset * n_plane + plane)
    place = (slot * n_z * n_plane + rank) * capacity + position
    hits = (place[:, None] == jnp.arange(places, dtype=jnp.int32)[None, :]).reshape(tok_dev, top_k, places)
    gather = jnp.sum(hits.astype(jnp.bfloat16), axis=1)
    mixing = jnp.sum(jnp.where(hits, route_weights[:, :, None], 0.0), axis=1)

    other = pair_swap(tokens, "zh")
    low, high = pick(half == 0, tokens, other)
    features = jnp.concatenate([low, high], axis=1)
    outgoing = lax.dot_general(
        gather, features, (((0,), (0,)), ((), ())), preferred_element_type=jnp.float32
    ).astype(jnp.bfloat16)

    half_rows = places // exp_dev
    wide = 2 * width
    first = outgoing[:half_rows].reshape(n_plane, half_rows // n_plane, wide)
    second = outgoing[half_rows:].reshape(n_z, half_rows // n_z, wide)
    first = plane_a2a(first)
    second = ring_out(second)
    first = first.reshape(n_plane, n_z, capacity, wide).transpose(1, 0, 2, 3)
    second = second.reshape(n_z, n_plane, capacity, wide).transpose(1, 0, 2, 3)
    first = ring_out(first.reshape(n_z, half_rows // n_z, wide))
    second = plane_a2a(second.reshape(n_plane, half_rows // n_plane, wide))
    arrived = [first.reshape(half_rows, wide), second.reshape(half_rows, wide)]

    mine = jnp.stack(arrived)
    theirs = pair_swap(mine, "core")
    even, odd = pick(core == 0, mine, theirs)
    rows = jnp.concatenate(
        [even[..., :width], odd[..., :width], even[..., width:], odd[..., width:]], axis=-1
    )
    projected = jnp.einsum("srd,sdgf->srgf", rows, gate_up, preferred_element_type=jnp.float32)
    hidden = (jax.nn.silu(projected[:, :, 0]) * projected[:, :, 1]).astype(jnp.bfloat16)
    partial = jnp.einsum("srf,sfd->srd", hidden, down, preferred_element_type=jnp.float32).astype(
        jnp.bfloat16
    )
    part_even = jnp.concatenate([partial[..., cut[0]], partial[..., cut[2]]], axis=-1)
    part_odd = jnp.concatenate([partial[..., cut[1]], partial[..., cut[3]]], axis=-1)
    keep, send = pick(core == 0, part_even, part_odd)
    paired = (keep.astype(jnp.float32) + pair_swap(send, "core").astype(jnp.float32)).astype(jnp.bfloat16)

    first = ring_back(paired[0].reshape(n_z, half_rows // n_z, wide))
    second = plane_a2a(paired[1].reshape(n_plane, half_rows // n_plane, wide))
    first = first.reshape(n_z, n_plane, capacity, wide).transpose(1, 0, 2, 3)
    second = second.reshape(n_plane, n_z, capacity, wide).transpose(1, 0, 2, 3)
    first = plane_a2a(first.reshape(n_plane, half_rows // n_plane, wide))
    second = ring_back(second.reshape(n_z, half_rows // n_z, wide))
    returned = jnp.concatenate([first.reshape(half_rows, wide), second.reshape(half_rows, wide)])
    weighted = jnp.dot(
        mixing,
        returned.astype(jnp.float32),
        precision=lax.Precision.HIGHEST,
        preferred_element_type=jnp.float32,
    )
    own, away = pick(half == 0, weighted[:, :width], weighted[:, width:])
    return (own + pair_swap(away.astype(jnp.bfloat16), "zh").astype(jnp.float32)).astype(jnp.bfloat16)


def solution(mesh):
    rep_size, ep_size = mesh.devices.shape
    side = round(ep_size ** (1 / 3))
    shape = (2, rep_size // 2, side, side, side)
    grid = Mesh(np.asarray(mesh.devices).reshape(shape), REP_AXES + EP_AXES)
    return jax.shard_map(
        shards,
        mesh=grid,
        in_specs=(
            P(EP_AXES, REP_AXES),
            P(EP_AXES, None),
            P(EP_AXES, None),
            P(),
            P(EP_AXES, None, None, REP_AXES),
            P(EP_AXES, REP_AXES, None),
        ),
        out_specs=P(EP_AXES, REP_AXES),
        check_vma=False,
    )
```

```python
import jax
import jax.numpy as jnp
import numpy as np
from jax import lax
from jax.sharding import Mesh
from jax.sharding import PartitionSpec as P

EP_AXES = ("z", "y", "x")
REP_AXES = ("zh", "core")
RING = ("zh", "z")
PLANE = ("y", "x")


def pair_swap(value, axis):
    return lax.ppermute(value, axis, [(0, 1), (1, 0)])


def ring_shift(value, shift):
    size = lax.axis_size(RING)
    return lax.ppermute(value, RING, [(i, (i + shift) % size) for i in range(size)])


def plane_a2a(value):
    return lax.all_to_all(value, PLANE, 0, 0, tiled=True)


def ring_out(chunks):
    cut = chunks.shape[1] // 2
    far = [ring_shift(chunks[2, :cut], 2), ring_shift(chunks[2, cut:], -2)]
    return [chunks[0], ring_shift(chunks[1], 1), far, ring_shift(chunks[3], -1)]


def ring_back(chunks):
    cut = chunks.shape[1] // 2
    far = [ring_shift(chunks[2, :cut], -2), ring_shift(chunks[2, cut:], 2)]
    return [chunks[0], ring_shift(chunks[1], -1), far, ring_shift(chunks[3], 1)]


def joined(pieces, shape, axis):
    pieces = [jnp.concatenate(piece) if isinstance(piece, list) else piece for piece in pieces]
    return jnp.stack([piece.reshape(shape) for piece in pieces], axis=axis)


def pick(flag, first, second):
    return jnp.where(flag, first, second), jnp.where(flag, second, first)


def holder_of(swap_plan, exp_dev):
    ep_size = swap_plan.shape[0]
    slot = jnp.arange(ep_size * exp_dev, dtype=jnp.int32)
    partner = jnp.repeat(swap_plan[:, 0], exp_dev)
    given = jnp.repeat(swap_plan[:, 1], exp_dev)
    choose = (partner[:, None] == jnp.arange(ep_size, dtype=jnp.int32)[None, :]).astype(jnp.float32)
    partner_given = jnp.dot(choose, swap_plan[:, 1].astype(jnp.float32)).astype(jnp.int32)
    moved = (partner != slot // exp_dev) & (slot % exp_dev == given)
    return jnp.where(moved, partner * exp_dev + partner_given, slot)


def shards(tokens, route_ids, route_weights, swap_plan, gate_up, down):
    n_z = lax.axis_size("z")
    n_plane = lax.axis_size("y") * lax.axis_size("x")
    ep_size = n_z * n_plane
    core = lax.axis_index("core")
    half = lax.axis_index("zh")
    exp_dev = gate_up.shape[0]
    experts = exp_dev * ep_size
    tok_dev, top_k = route_ids.shape
    routed = tok_dev * top_k
    capacity = max(2, (routed * 3 + 2 * experts - 1) // (2 * experts))
    places = experts * capacity
    width = tokens.shape[1]
    cut = [slice(i * width, (i + 1) * width) for i in range(4)]

    holder = holder_of(swap_plan, exp_dev)
    catalog = jnp.arange(experts, dtype=jnp.int32)
    named = (route_ids.reshape(routed)[:, None] == catalog[None, :]).astype(jnp.float32)
    owners = jnp.dot(named, holder.astype(jnp.float32)).astype(jnp.int32)
    one_hot = (owners[:, None] == catalog[None, :]).astype(jnp.float32)
    earlier = (jnp.arange(routed)[:, None] > jnp.arange(routed)[None, :]).astype(jnp.float32)
    before = jnp.dot(earlier, one_hot, preferred_element_type=jnp.float32)
    position = jnp.sum(before * one_hot, axis=1).astype(jnp.int32)
    device = owners // exp_dev
    plane = device % n_plane
    offset = (device // n_plane - lax.axis_index("z")) % n_z
    slot = owners % exp_dev
    rank = jnp.where(slot == 0, plane * n_z + offset, offset * n_plane + plane)
    place = (slot * n_z * n_plane + rank) * capacity + position
    hits = (place[:, None] == jnp.arange(places, dtype=jnp.int32)[None, :]).reshape(tok_dev, top_k, places)
    gather = jnp.sum(hits.astype(jnp.bfloat16), axis=1)
    mixing = jnp.sum(jnp.where(hits, route_weights[:, :, None], 0.0), axis=1)

    other = pair_swap(tokens, "zh")
    low, high = pick(half == 0, tokens, other)
    features = jnp.concatenate([low, high], axis=1)
    outgoing = lax.dot_general(
        gather, features, (((0,), (0,)), ((), ())), preferred_element_type=jnp.float32
    ).astype(jnp.bfloat16)

    half_rows = places // exp_dev
    wide = 2 * width
    first = outgoing[:half_rows].reshape(n_plane, half_rows // n_plane, wide)
    second = outgoing[half_rows:].reshape(n_z, half_rows // n_z, wide)
    first = plane_a2a(first)
    second = joined(ring_out(second), (n_plane, capacity, wide), 1)
    first = first.reshape(n_plane, n_z, capacity, wide).transpose(1, 0, 2, 3)
    first = joined(ring_out(first.reshape(n_z, half_rows // n_z, wide)), (half_rows // n_z, wide), 0)
    second = plane_a2a(second.reshape(n_plane, half_rows // n_plane, wide))
    arrived = [first.reshape(half_rows, wide), second.reshape(half_rows, wide)]

    mine = jnp.stack(arrived)
    theirs = pair_swap(mine, "core")
    even, odd = pick(core == 0, mine, theirs)
    rows = jnp.concatenate(
        [even[..., :width], odd[..., :width], even[..., width:], odd[..., width:]], axis=-1
    )
    projected = jnp.einsum("srd,sdgf->srgf", rows, gate_up, preferred_element_type=jnp.float32)
    hidden = (jax.nn.silu(projected[:, :, 0]) * projected[:, :, 1]).astype(jnp.bfloat16)
    partial = jnp.einsum("srf,sfd->srd", hidden, down, preferred_element_type=jnp.float32).astype(
        jnp.bfloat16
    )
    part_even = jnp.concatenate([partial[..., cut[0]], partial[..., cut[2]]], axis=-1)
    part_odd = jnp.concatenate([partial[..., cut[1]], partial[..., cut[3]]], axis=-1)
    keep, send = pick(core == 0, part_even, part_odd)
    paired = (keep.astype(jnp.float32) + pair_swap(send, "core").astype(jnp.float32)).astype(jnp.bfloat16)

    first = joined(ring_back(paired[0].reshape(n_z, half_rows // n_z, wide)), (n_plane, capacity, wide), 1)
    second = plane_a2a(paired[1].reshape(n_plane, half_rows // n_plane, wide))
    second = second.reshape(n_plane, n_z, capacity, wide).transpose(1, 0, 2, 3)
    first = plane_a2a(first.reshape(n_plane, half_rows // n_plane, wide))
    second = joined(ring_back(second.reshape(n_z, half_rows // n_z, wide)), (half_rows // n_z, wide), 0)
    returned = jnp.concatenate([first.reshape(half_rows, wide), second.reshape(half_rows, wide)])
    weighted = jnp.dot(
        mixing,
        returned.astype(jnp.float32),
        precision=lax.Precision.HIGHEST,
        preferred_element_type=jnp.float32,
    )
    own, away = pick(half == 0, weighted[:, :width], weighted[:, width:])
    return (own + pair_swap(away.astype(jnp.bfloat16), "zh").astype(jnp.float32)).astype(jnp.bfloat16)


def solution(mesh):
    rep_size, ep_size = mesh.devices.shape
    side = round(ep_size ** (1 / 3))
    shape = (2, rep_size // 2, side, side, side)
    grid = Mesh(np.asarray(mesh.devices).reshape(shape), REP_AXES + EP_AXES)
    return jax.shard_map(
        shards,
        mesh=grid,
        in_specs=(
            P(EP_AXES, REP_AXES),
            P(EP_AXES, None),
            P(EP_AXES, None),
            P(),
            P(EP_AXES, None, None, REP_AXES),
            P(EP_AXES, REP_AXES, None),
        ),
        out_specs=P(EP_AXES, REP_AXES),
        check_vma=False,
    )
```

```python
import jax
import jax.numpy as jnp
import numpy as np
from jax import lax
from jax.sharding import Mesh
from jax.sharding import PartitionSpec as P

EP_AXES = ("z", "y", "x")
REP_AXES = ("zh", "core")
RING = ("zh", "z")
PLANE = ("y", "x")


def pair_swap(value, axis):
    return lax.ppermute(value, axis, [(0, 1), (1, 0)])


def ring_shift(value, shift):
    size = lax.axis_size(RING)
    return lax.ppermute(value, RING, [(i, (i + shift) % size) for i in range(size)])


def plane_a2a(value):
    return lax.all_to_all(value, PLANE, 0, 0, tiled=True)


def ring_out(chunks):
    cut = chunks.shape[1] // 2
    far = [ring_shift(chunks[2, :cut], 2), ring_shift(chunks[2, cut:], -2)]
    return [chunks[0], ring_shift(chunks[1], 1), far, ring_shift(chunks[3], -1)]


def ring_back(chunks):
    cut = chunks.shape[1] // 2
    far = [ring_shift(chunks[2, :cut], -2), ring_shift(chunks[2, cut:], 2)]
    return [chunks[0], ring_shift(chunks[1], -1), far, ring_shift(chunks[3], 1)]


def joined(pieces, shape, axis):
    pieces = [jnp.concatenate(piece) if isinstance(piece, list) else piece for piece in pieces]
    return jnp.stack([piece.reshape(shape) for piece in pieces], axis=axis)


def pick(flag, first, second):
    return jnp.where(flag, first, second), jnp.where(flag, second, first)


def holder_of(swap_plan, exp_dev):
    ep_size = swap_plan.shape[0]
    slot = jnp.arange(ep_size * exp_dev, dtype=jnp.int32)
    partner = jnp.repeat(swap_plan[:, 0], exp_dev)
    given = jnp.repeat(swap_plan[:, 1], exp_dev)
    choose = (partner[:, None] == jnp.arange(ep_size, dtype=jnp.int32)[None, :]).astype(jnp.float32)
    partner_given = jnp.dot(choose, swap_plan[:, 1].astype(jnp.float32)).astype(jnp.int32)
    moved = (partner != slot // exp_dev) & (slot % exp_dev == given)
    return jnp.where(moved, partner * exp_dev + partner_given, slot)


def shards(tokens, route_ids, route_weights, swap_plan, gate_up, down):
    n_z = lax.axis_size("z")
    n_plane = lax.axis_size("y") * lax.axis_size("x")
    ep_size = n_z * n_plane
    core = lax.axis_index("core")
    half = lax.axis_index("zh")
    exp_dev = gate_up.shape[0]
    experts = exp_dev * ep_size
    tok_dev, top_k = route_ids.shape
    routed = tok_dev * top_k
    capacity = max(2, (routed * 3 + 2 * experts - 1) // (2 * experts))
    places = experts * capacity
    width = tokens.shape[1]
    cut = [slice(i * width, (i + 1) * width) for i in range(4)]

    holder = holder_of(swap_plan, exp_dev)
    catalog = jnp.arange(experts, dtype=jnp.int32)
    named = (route_ids.reshape(routed)[:, None] == catalog[None, :]).astype(jnp.float32)
    owners = jnp.dot(named, holder.astype(jnp.float32)).astype(jnp.int32)
    one_hot = (owners[:, None] == catalog[None, :]).astype(jnp.float32)
    earlier = (jnp.arange(routed)[:, None] > jnp.arange(routed)[None, :]).astype(jnp.float32)
    before = jnp.dot(earlier, one_hot, preferred_element_type=jnp.float32)
    position = jnp.sum(before * one_hot, axis=1).astype(jnp.int32)
    device = owners // exp_dev
    plane = device % n_plane
    offset = (device // n_plane - lax.axis_index("z")) % n_z
    slot = owners % exp_dev
    rank = jnp.where(slot == 0, plane * n_z + offset, offset * n_plane + plane)
    place = (slot * n_z * n_plane + rank) * capacity + position
    hits = (place[:, None] == jnp.arange(places, dtype=jnp.int32)[None, :]).reshape(tok_dev, top_k, places)
    gather = jnp.sum(hits.astype(jnp.bfloat16), axis=1)
    mixing = jnp.sum(jnp.where(hits, route_weights[:, :, None], 0.0), axis=1)

    gather, mixing, tokens = lax.optimization_barrier((gather, mixing, tokens))
    other = pair_swap(tokens, "zh")
    low, high = pick(half == 0, tokens, other)
    features = jnp.concatenate([low, high], axis=1)
    outgoing = lax.dot_general(
        gather, features, (((0,), (0,)), ((), ())), preferred_element_type=jnp.float32
    ).astype(jnp.bfloat16)

    half_rows = places // exp_dev
    wide = 2 * width
    first = outgoing[:half_rows].reshape(n_plane, half_rows // n_plane, wide)
    second = outgoing[half_rows:].reshape(n_z, half_rows // n_z, wide)
    first = plane_a2a(first)
    second = joined(ring_out(second), (n_plane, capacity, wide), 1)
    first = first.reshape(n_plane, n_z, capacity, wide).transpose(1, 0, 2, 3)
    first = joined(ring_out(first.reshape(n_z, half_rows // n_z, wide)), (half_rows // n_z, wide), 0)
    second = plane_a2a(second.reshape(n_plane, half_rows // n_plane, wide))
    arrived = [first.reshape(half_rows, wide), second.reshape(half_rows, wide)]

    mine = jnp.stack(arrived)
    theirs = pair_swap(mine, "core")
    even, odd = pick(core == 0, mine, theirs)
    rows = jnp.concatenate(
        [even[..., :width], odd[..., :width], even[..., width:], odd[..., width:]], axis=-1
    )
    projected = jnp.einsum("srd,sdgf->srgf", rows, gate_up, preferred_element_type=jnp.float32)
    hidden = (jax.nn.silu(projected[:, :, 0]) * projected[:, :, 1]).astype(jnp.bfloat16)
    partial = jnp.einsum("srf,sfd->srd", hidden, down, preferred_element_type=jnp.float32).astype(
        jnp.bfloat16
    )
    part_even = jnp.concatenate([partial[..., cut[0]], partial[..., cut[2]]], axis=-1)
    part_odd = jnp.concatenate([partial[..., cut[1]], partial[..., cut[3]]], axis=-1)
    keep, send = pick(core == 0, part_even, part_odd)
    paired = (keep.astype(jnp.float32) + pair_swap(send, "core").astype(jnp.float32)).astype(jnp.bfloat16)

    first = joined(ring_back(paired[0].reshape(n_z, half_rows // n_z, wide)), (n_plane, capacity, wide), 1)
    second = plane_a2a(paired[1].reshape(n_plane, half_rows // n_plane, wide))
    second = second.reshape(n_plane, n_z, capacity, wide).transpose(1, 0, 2, 3)
    first = plane_a2a(first.reshape(n_plane, half_rows // n_plane, wide))
    second = joined(ring_back(second.reshape(n_z, half_rows // n_z, wide)), (half_rows // n_z, wide), 0)
    returned = jnp.concatenate([first.reshape(half_rows, wide), second.reshape(half_rows, wide)])
    weighted = jnp.dot(
        mixing,
        returned.astype(jnp.float32),
        precision=lax.Precision.HIGHEST,
        preferred_element_type=jnp.float32,
    )
    own, away = pick(half == 0, weighted[:, :width], weighted[:, width:])
    return (own + pair_swap(away.astype(jnp.bfloat16), "zh").astype(jnp.float32)).astype(jnp.bfloat16)


def solution(mesh):
    rep_size, ep_size = mesh.devices.shape
    side = round(ep_size ** (1 / 3))
    shape = (2, rep_size // 2, side, side, side)
    grid = Mesh(np.asarray(mesh.devices).reshape(shape), REP_AXES + EP_AXES)
    return jax.shard_map(
        shards,
        mesh=grid,
        in_specs=(
            P(EP_AXES, REP_AXES),
            P(EP_AXES, None),
            P(EP_AXES, None),
            P(),
            P(EP_AXES, None, None, REP_AXES),
            P(EP_AXES, REP_AXES, None),
        ),
        out_specs=P(EP_AXES, REP_AXES),
        check_vma=False,
    )
```

```python
import jax
import jax.numpy as jnp
import numpy as np
from jax import lax
from jax.sharding import Mesh
from jax.sharding import PartitionSpec as P

EP_AXES = ("z", "y", "x")
REP_AXES = ("zh", "core")
RING = ("zh", "z")
PLANE = ("y", "x")


def pair_swap(value, axis):
    return lax.ppermute(value, axis, [(0, 1), (1, 0)])


def ring_shift(value, shift):
    size = lax.axis_size(RING)
    return lax.ppermute(value, RING, [(i, (i + shift) % size) for i in range(size)])


def plane_a2a(value):
    return lax.all_to_all(value, PLANE, 0, 0, tiled=True)


def ring_out(chunks):
    cut = chunks.shape[1] // 2
    far = [ring_shift(chunks[2, :cut], 2), ring_shift(chunks[2, cut:], -2)]
    return [chunks[0], ring_shift(chunks[1], 1), far, ring_shift(chunks[3], -1)]


def ring_back(chunks):
    cut = chunks.shape[1] // 2
    far = [ring_shift(chunks[2, :cut], -2), ring_shift(chunks[2, cut:], 2)]
    return [chunks[0], ring_shift(chunks[1], -1), far, ring_shift(chunks[3], 1)]


def joined(pieces, shape, axis):
    pieces = [jnp.concatenate(piece) if isinstance(piece, list) else piece for piece in pieces]
    return jnp.stack([piece.reshape(shape) for piece in pieces], axis=axis)


def pick(flag, first, second):
    return jnp.where(flag, first, second), jnp.where(flag, second, first)


def holder_of(swap_plan, exp_dev):
    ep_size = swap_plan.shape[0]
    slot = jnp.arange(ep_size * exp_dev, dtype=jnp.int32)
    partner = jnp.repeat(swap_plan[:, 0], exp_dev)
    given = jnp.repeat(swap_plan[:, 1], exp_dev)
    choose = (partner[:, None] == jnp.arange(ep_size, dtype=jnp.int32)[None, :]).astype(jnp.float32)
    partner_given = jnp.dot(choose, swap_plan[:, 1].astype(jnp.float32)).astype(jnp.int32)
    moved = (partner != slot // exp_dev) & (slot % exp_dev == given)
    return jnp.where(moved, partner * exp_dev + partner_given, slot)


def shards(tokens, route_ids, route_weights, swap_plan, gate_up, down):
    n_z = lax.axis_size("z")
    n_plane = lax.axis_size("y") * lax.axis_size("x")
    ep_size = n_z * n_plane
    core = lax.axis_index("core")
    half = lax.axis_index("zh")
    exp_dev = gate_up.shape[0]
    experts = exp_dev * ep_size
    tok_dev, top_k = route_ids.shape
    routed = tok_dev * top_k
    capacity = max(2, (routed * 3 + 2 * experts - 1) // (2 * experts))
    places = experts * capacity
    width = tokens.shape[1]
    cut = [slice(i * width, (i + 1) * width) for i in range(4)]

    holder = holder_of(swap_plan, exp_dev)
    catalog = jnp.arange(experts, dtype=jnp.int32)
    named = (route_ids.reshape(routed)[:, None] == catalog[None, :]).astype(jnp.float32)
    owners = jnp.dot(named, holder.astype(jnp.float32)).astype(jnp.int32)
    one_hot = (owners[:, None] == catalog[None, :]).astype(jnp.float32)
    earlier = (jnp.arange(routed)[:, None] > jnp.arange(routed)[None, :]).astype(jnp.float32)
    before = jnp.dot(earlier, one_hot, preferred_element_type=jnp.float32)
    position = jnp.sum(before * one_hot, axis=1).astype(jnp.int32)
    device = owners // exp_dev
    plane = device % n_plane
    offset = (device // n_plane - lax.axis_index("z")) % n_z
    slot = owners % exp_dev
    rank = jnp.where(slot == 0, plane * n_z + offset, offset * n_plane + plane)
    place = (slot * n_z * n_plane + rank) * capacity + position
    hits = (place[:, None] == jnp.arange(places, dtype=jnp.int32)[None, :]).reshape(tok_dev, top_k, places)
    gather = jnp.sum(hits.astype(jnp.bfloat16), axis=1)
    mixing = jnp.sum(jnp.where(hits, route_weights[:, :, None], 0.0), axis=1)

    other = pair_swap(tokens, "zh")
    low, high = pick(half == 0, tokens, other)
    features = jnp.concatenate([low, high], axis=1)
    outgoing = lax.dot_general(
        gather, features, (((0,), (0,)), ((), ())), preferred_element_type=jnp.float32
    ).astype(jnp.bfloat16)

    half_rows = places // exp_dev
    wide = 2 * width
    first = outgoing[:half_rows].reshape(n_plane, half_rows // n_plane, wide)
    second = outgoing[half_rows:].reshape(n_z, half_rows // n_z, wide)
    first = plane_a2a(first)
    second = joined(ring_out(second), (n_plane, capacity, wide), 1)
    first = first.reshape(n_plane, n_z, capacity, wide).transpose(1, 0, 2, 3)
    first = joined(ring_out(first.reshape(n_z, half_rows // n_z, wide)), (half_rows // n_z, wide), 0)
    second = plane_a2a(second.reshape(n_plane, half_rows // n_plane, wide))
    arrived = [first.reshape(half_rows, wide), second.reshape(half_rows, wide)]

    mine = jnp.stack(arrived)
    theirs = pair_swap(mine, "core")
    even, odd = pick(core == 0, mine, theirs)
    rows = jnp.concatenate(
        [even[..., :width], odd[..., :width], even[..., width:], odd[..., width:]], axis=-1
    )
    projected = jnp.einsum("srd,sdgf->srgf", rows, gate_up, preferred_element_type=jnp.float32)
    hidden = (jax.nn.silu(projected[:, :, 0]) * projected[:, :, 1]).astype(jnp.bfloat16)
    partial = jnp.einsum("srf,sfd->srd", hidden, down, preferred_element_type=jnp.float32).astype(
        jnp.bfloat16
    )
    part_even = jnp.concatenate([partial[..., cut[0]], partial[..., cut[2]]], axis=-1)
    part_odd = jnp.concatenate([partial[..., cut[1]], partial[..., cut[3]]], axis=-1)
    keep, send = pick(core == 0, part_even, part_odd)
    paired = (keep.astype(jnp.float32) + pair_swap(send, "core").astype(jnp.float32)).astype(jnp.bfloat16)

    first = joined(ring_back(paired[0].reshape(n_z, half_rows // n_z, wide)), (n_plane, capacity, wide), 1)
    second = plane_a2a(paired[1].reshape(n_plane, half_rows // n_plane, wide))
    second = second.reshape(n_plane, n_z, capacity, wide).transpose(1, 0, 2, 3)
    first = plane_a2a(first.reshape(n_plane, half_rows // n_plane, wide))
    second = joined(ring_back(second.reshape(n_z, half_rows // n_z, wide)), (half_rows // n_z, wide), 0)
    returned = jnp.concatenate([first.reshape(half_rows, wide), second.reshape(half_rows, wide)])
    high = mixing.astype(jnp.bfloat16)
    low = (mixing - high.astype(jnp.float32)).astype(jnp.bfloat16)
    weighted = jnp.dot(high, returned, preferred_element_type=jnp.float32) + jnp.dot(
        low, returned, preferred_element_type=jnp.float32
    )
    own, away = pick(half == 0, weighted[:, :width], weighted[:, width:])
    return (own + pair_swap(away.astype(jnp.bfloat16), "zh").astype(jnp.float32)).astype(jnp.bfloat16)


def solution(mesh):
    rep_size, ep_size = mesh.devices.shape
    side = round(ep_size ** (1 / 3))
    shape = (2, rep_size // 2, side, side, side)
    grid = Mesh(np.asarray(mesh.devices).reshape(shape), REP_AXES + EP_AXES)
    return jax.shard_map(
        shards,
        mesh=grid,
        in_specs=(
            P(EP_AXES, REP_AXES),
            P(EP_AXES, None),
            P(EP_AXES, None),
            P(),
            P(EP_AXES, None, None, REP_AXES),
            P(EP_AXES, REP_AXES, None),
        ),
        out_specs=P(EP_AXES, REP_AXES),
        check_vma=False,
    )
```

```python
import jax
import jax.numpy as jnp
import numpy as np
from jax import lax
from jax.sharding import Mesh
from jax.sharding import PartitionSpec as P

EP_AXES = ("z", "y", "x")
REP_AXES = ("zh", "core")
RING = ("zh", "z")
PLANE = ("y", "x")


def pair_swap(value, axis):
    return lax.ppermute(value, axis, [(0, 1), (1, 0)])


def ring_shift(value, shift):
    size = lax.axis_size(RING)
    return lax.ppermute(value, RING, [(i, (i + shift) % size) for i in range(size)])


def plane_a2a(value):
    return lax.all_to_all(value, PLANE, 0, 0, tiled=True)


def ring_out(chunks):
    cut = chunks.shape[1] // 2
    far = [ring_shift(chunks[2, :cut], 2), ring_shift(chunks[2, cut:], -2)]
    return [chunks[0], ring_shift(chunks[1], 1), far, ring_shift(chunks[3], -1)]


def ring_back(chunks):
    cut = chunks.shape[1] // 2
    far = [ring_shift(chunks[2, :cut], -2), ring_shift(chunks[2, cut:], 2)]
    return [chunks[0], ring_shift(chunks[1], -1), far, ring_shift(chunks[3], 1)]


def joined(pieces, shape, axis):
    pieces = [jnp.concatenate(piece) if isinstance(piece, list) else piece for piece in pieces]
    return jnp.stack([piece.reshape(shape) for piece in pieces], axis=axis)


def pick(flag, first, second):
    return jnp.where(flag, first, second), jnp.where(flag, second, first)


def holder_of(swap_plan, exp_dev):
    ep_size = swap_plan.shape[0]
    slot = jnp.arange(ep_size * exp_dev, dtype=jnp.int32)
    partner = jnp.repeat(swap_plan[:, 0], exp_dev)
    given = jnp.repeat(swap_plan[:, 1], exp_dev)
    choose = (partner[:, None] == jnp.arange(ep_size, dtype=jnp.int32)[None, :]).astype(jnp.float32)
    partner_given = jnp.dot(choose, swap_plan[:, 1].astype(jnp.float32)).astype(jnp.int32)
    moved = (partner != slot // exp_dev) & (slot % exp_dev == given)
    return jnp.where(moved, partner * exp_dev + partner_given, slot)


def shards(tokens, route_ids, route_weights, swap_plan, gate_up, down):
    n_z = lax.axis_size("z")
    n_plane = lax.axis_size("y") * lax.axis_size("x")
    ep_size = n_z * n_plane
    core = lax.axis_index("core")
    half = lax.axis_index("zh")
    exp_dev = gate_up.shape[0]
    experts = exp_dev * ep_size
    tok_dev, top_k = route_ids.shape
    routed = tok_dev * top_k
    capacity = max(2, (routed * 3 + 2 * experts - 1) // (2 * experts))
    places = experts * capacity
    width = tokens.shape[1]
    cut = [slice(i * width, (i + 1) * width) for i in range(4)]

    holder = holder_of(swap_plan, exp_dev)
    catalog = jnp.arange(experts, dtype=jnp.int32)
    named = (route_ids.reshape(routed)[:, None] == catalog[None, :]).astype(jnp.float32)
    owners = jnp.dot(named, holder.astype(jnp.float32)).astype(jnp.int32)
    one_hot = (owners[:, None] == catalog[None, :]).astype(jnp.float32)
    earlier = (jnp.arange(routed)[:, None] > jnp.arange(routed)[None, :]).astype(jnp.float32)
    before = jnp.dot(earlier, one_hot, preferred_element_type=jnp.float32)
    position = jnp.sum(before * one_hot, axis=1).astype(jnp.int32)
    device = owners // exp_dev
    plane = device % n_plane
    offset = (device // n_plane - lax.axis_index("z")) % n_z
    slot = owners % exp_dev
    rank = jnp.where(slot == 0, plane * n_z + offset, offset * n_plane + plane)
    place = (slot * n_z * n_plane + rank) * capacity + position
    hits = (place[:, None] == jnp.arange(places, dtype=jnp.int32)[None, :]).reshape(tok_dev, top_k, places)
    gather = jnp.sum(hits.astype(jnp.bfloat16), axis=1)
    mixing = jnp.sum(jnp.where(hits, route_weights[:, :, None], 0.0), axis=1)

    other = pair_swap(tokens, "zh")
    low, high = pick(half == 0, tokens, other)
    features = jnp.concatenate([low, high], axis=1)
    outgoing = lax.dot_general(
        gather, features, (((0,), (0,)), ((), ())), preferred_element_type=jnp.float32
    ).astype(jnp.bfloat16)

    half_rows = places // exp_dev
    wide = 2 * width
    first = outgoing[:half_rows].reshape(n_plane, half_rows // n_plane, wide)
    second = outgoing[half_rows:].reshape(n_z, half_rows // n_z, wide)
    first = plane_a2a(first)
    second = joined(ring_out(second), (n_plane, capacity, wide), 1)
    first = first.reshape(n_plane, n_z, capacity, wide).transpose(1, 0, 2, 3)
    first = joined(ring_out(first.reshape(n_z, half_rows // n_z, wide)), (half_rows // n_z, wide), 0)
    second = plane_a2a(second.reshape(n_plane, half_rows // n_plane, wide))
    arrived = [first.reshape(half_rows, wide), second.reshape(half_rows, wide)]

    mine = jnp.stack(arrived)
    theirs = pair_swap(mine, "core")
    even, odd = pick(core == 0, mine, theirs)
    rows = jnp.concatenate(
        [even[..., :width], odd[..., :width], even[..., width:], odd[..., width:]], axis=-1
    )
    projected = jnp.einsum("srd,sdgf->srgf", rows, gate_up, preferred_element_type=jnp.float32)
    hidden = (jax.nn.silu(projected[:, :, 0]) * projected[:, :, 1]).astype(jnp.bfloat16)
    partial = jnp.einsum("srf,sfd->srd", hidden, down, preferred_element_type=jnp.float32).astype(
        jnp.bfloat16
    )
    part_even = jnp.concatenate([partial[..., cut[0]], partial[..., cut[2]]], axis=-1)
    part_odd = jnp.concatenate([partial[..., cut[1]], partial[..., cut[3]]], axis=-1)
    keep, send = pick(core == 0, part_even, part_odd)
    paired = (keep.astype(jnp.float32) + pair_swap(send, "core").astype(jnp.float32)).astype(jnp.bfloat16)

    first = joined(ring_back(paired[0].reshape(n_z, half_rows // n_z, wide)), (n_plane, capacity, wide), 1)
    second = plane_a2a(paired[1].reshape(n_plane, half_rows // n_plane, wide))
    second = second.reshape(n_plane, n_z, capacity, wide).transpose(1, 0, 2, 3)
    first = plane_a2a(first.reshape(n_plane, half_rows // n_plane, wide))
    second = joined(ring_back(second.reshape(n_z, half_rows // n_z, wide)), (half_rows // n_z, wide), 0)
    returned = jnp.concatenate([first.reshape(half_rows, wide), second.reshape(half_rows, wide)])
    weighted = jnp.dot(
        mixing,
        returned.astype(jnp.float32),
        precision=lax.Precision.HIGHEST,
        preferred_element_type=jnp.float32,
    )
    own = lax.dynamic_slice_in_dim(weighted, half * width, width, axis=1)
    away = lax.dynamic_slice_in_dim(weighted, (1 - half) * width, width, axis=1)
    return (own + pair_swap(away.astype(jnp.bfloat16), "zh").astype(jnp.float32)).astype(jnp.bfloat16)


def solution(mesh):
    rep_size, ep_size = mesh.devices.shape
    side = round(ep_size ** (1 / 3))
    shape = (2, rep_size // 2, side, side, side)
    grid = Mesh(np.asarray(mesh.devices).reshape(shape), REP_AXES + EP_AXES)
    return jax.shard_map(
        shards,
        mesh=grid,
        in_specs=(
            P(EP_AXES, REP_AXES),
            P(EP_AXES, None),
            P(EP_AXES, None),
            P(),
            P(EP_AXES, None, None, REP_AXES),
            P(EP_AXES, REP_AXES, None),
        ),
        out_specs=P(EP_AXES, REP_AXES),
        check_vma=False,
    )
```
